512 devices in a mesh: px: 32 (over y, x, core), py: 16 (over z).
Axes of the slice: x: 4, y: 4, z: 16, core: 2. Of those that a mesh axis runs over, the one named last changes fastest.
Arguments:
- start_vecs: float32 [8192, 64, 128], P(('px', 'py')), may hold values from -6 to 6
- local_tiles: bfloat16 [8192, 4, 128, 128], P(('px', 'py')), may hold values from -0.078125 to 0.078125
- local_cols: int32 [8192, 4], P(('px', 'py')), may hold values from 0 to 15
- halo_tiles: bfloat16 [8192, 128, 128], P(('px', 'py')), may hold values from -0.078125 to 0.078125
- halo_slot: int32 [8192], P(('px', 'py')), may hold values from 0 to 7
- boundary: int32 [2048, 2], P(('px', 'py')), may hold values from 0 to 15
Outputs:
- filtered: float32 [8192, 64, 128], P(('px', 'py'))
- gram_matrix: float32 [64, 64], replicated
The draws below stay inside these ranges and needn't reach their ends.
Inputs may be any that keep to these rules, and one draw needn't show every extreme that they name: `local_cols`: local block indices within the partition. `boundary`: local block indices within the partition.
All inputs are finite; a program needn't handle non-finite values.
Results may differ from the reference program's by a relative error of at most 0.0055.
Values may be sent and summed in bfloat16 or wider, within the bound.
No kernel may reach another device: no remote copies, remote signals or barrier semaphores. Data moves between devices by JAX's collectives and lax.ppermute only.
A program may use at most 64 MiB of HBM per device.

```python
import math
import jax
import jax.numpy as jnp
from jax import lax

K = 64
BS = 128
RB = 16
TPR = 4
NB = 2
DEG = 9
NBLK = 8192
ROWS = 1048576
N_PX = 32
N_PY = 16
DEVICES = 512


def draw_start_vecs(key, part):
    key_own = jax.random.fold_in(key, 11)
    key_shared = jax.random.fold_in(key, 23)
    key_weight = jax.random.fold_in(key, 37)
    key_sign = jax.random.fold_in(key, 41)
    own_part = jax.random.normal(key_own, (NBLK, K, BS), jnp.float32)
    shared_field = jax.random.normal(key_shared, (NBLK, 1, BS), jnp.float32)
    magnitude = jnp.exp(jax.random.uniform(key_weight, (K,), jnp.float32, math.log(0.5), math.log(1.5)))
    sign_flip = (2 * jax.random.randint(key_sign, (K,), 0, 2) - 1).astype(jnp.float32)
    mixed = own_part + (sign_flip * magnitude)[None, :, None] * shared_field
    return jnp.clip(mixed, -6.0, 6.0)


def set_ends(values, rng, least, high):
    shape = values.shape
    spot = [jax.random.randint(jax.random.fold_in(rng, axis), (), 0, shape[axis]) for axis in range(len(shape))]
    values = values.at[tuple(spot)].set(least)
    longest = shape.index(max(shape))
    spot[longest] = (spot[longest] + 1) % shape[longest]
    return values.at[tuple(spot)].set(high)


def block_scale(key, dims, shards, low, top_value):
    level, own = 1.0, jax.random.fold_in(key, 6)
    for axis_at, parts in shards:
        heights = jnp.exp(jax.random.uniform(jax.random.fold_in(own, axis_at), (parts,), jnp.float32, low / len(shards), top_value / len(shards)))
        level = level * jnp.repeat(heights, dims[axis_at] // parts).reshape([-1 if axis == axis_at else 1 for axis in range(len(dims))])
    return level


def bell_draw(key, shape, scale, limit, split=(), held_as=jnp.bfloat16):
    factor_of = block_scale(key, shape, split, -0.22, 0.18) if split else 1.0
    entries = jax.random.normal(key, shape, jnp.float32) * scale * factor_of
    return jnp.minimum(jnp.maximum(entries, -limit), limit).astype(held_as)


def setup_inputs(seed: int = 0) -> dict:
    key_list = jax.random.split(jax.random.key(seed), 7)
    start_vecs = draw_start_vecs(jax.random.fold_in(key_list[6], 71), 0)
    local_tiles = bell_draw(key_list[1], (NBLK, TPR, BS, BS), (8 * BS * (TPR + 1)) ** -0.5, 0.078125, ((0, 512),))
    local_cols = set_ends(jax.random.randint(key_list[2], (NBLK, TPR), 0, RB), jax.random.fold_in(key_list[2], 1), 0, RB - 1).astype(jnp.int32)
    halo_tiles = bell_draw(key_list[3], (NBLK, BS, BS), (8 * BS * (TPR + 1)) ** -0.5, 0.078125, ((0, 512),))
    halo_slot = set_ends(jax.random.randint(key_list[4], (NBLK,), 0, 4 * NB), jax.random.fold_in(key_list[4], 1), 0, (4 * NB) - 1).astype(jnp.int32)
    boundary = set_ends(jax.random.randint(key_list[5], (4 * DEVICES, NB), 0, RB), jax.random.fold_in(key_list[5], 1), 0, RB - 1).astype(jnp.int32)
    return {"start_vecs": start_vecs, "local_tiles": local_tiles, "local_cols": local_cols, "halo_tiles": halo_tiles, "halo_slot": halo_slot, "boundary": boundary}


def reference(start_vecs, local_tiles, local_cols, halo_tiles, halo_slot, boundary):
    tiles_dev = local_tiles.reshape(DEVICES, RB, TPR, BS, BS)
    cols_dev = local_cols.reshape(DEVICES, RB, TPR)
    halo_dev = halo_tiles.reshape(DEVICES, RB, BS, BS)
    slots_dev = halo_slot.reshape(DEVICES, RB)
    bound_dev = boundary.reshape(DEVICES, 4, NB)

    def per_device(pieces):
        blocks_one, recv_one, tile_set, col_set, halo_set, slot_set = pieces
        gathered = blocks_one[col_set].astype(jnp.float32)
        product = jnp.einsum('rtkj,rtij->rki', gathered, tile_set.astype(jnp.float32))
        coupled = jnp.einsum('rkj,rij->rki', recv_one[slot_set].astype(jnp.float32), halo_set.astype(jnp.float32))
        return product + coupled

    def operator_apply(current):
        rounded = current.astype(jnp.bfloat16)
        outgoing = jax.vmap(lambda blocks_one, picks: blocks_one[picks])(rounded, bound_dev)
        grid_view = outgoing.reshape(N_PX, N_PY, 4, NB, K, BS)
        received = jnp.concatenate([jnp.roll(grid_view[:, :, 0], 1, 0), jnp.roll(grid_view[:, :, 1], -1, 0), jnp.roll(grid_view[:, :, 2], 1, 1), jnp.roll(grid_view[:, :, 3], -1, 1)], axis=2)
        received = received.reshape(DEVICES, 4 * NB, K, BS)
        return lax.map(per_device, (rounded, received, tiles_dev, cols_dev, halo_dev, slots_dev))
    previous = start_vecs.reshape(DEVICES, RB, K, BS)
    current = operator_apply(previous)
    for degree_step in range(DEG - 1):
        previous, current = (current, 2.0 * operator_apply(current) - previous)
    squares = lax.optimization_barrier(jnp.sum(current * current, axis=(0, 1, 3)))
    scales = lax.rsqrt(squares / ROWS + 1e-06)
    filtered = current * scales[None, None, :, None]
    gram_matrix = jnp.einsum('drkj,drlj->kl', filtered, filtered, precision=lax.Precision.HIGHEST) / ROWS
    return (filtered.reshape(NBLK, K, BS), gram_matrix)
```

```python
import jax
import jax.numpy as jnp
from jax import lax
from jax.sharding import PartitionSpec as P

DEG = 9


def from_behind(value, axis, steps):
    count = lax.axis_size(axis)
    pairs = [(source, (source + steps) % count) for source in range(count)]
    return lax.ppermute(value, axis, pairs)


def butterfly_sum(value, axis):
    count = lax.axis_size(axis)
    stride = 1
    while stride < count:
        pairs = [(source, source ^ stride) for source in range(count)]
        value = value + lax.ppermute(value, axis, pairs)
        stride *= 2
    return value


def operator_apply(current, local_tiles, local_cols, halo_tiles, halo_slot, boundary):
    rounded = current.astype(jnp.bfloat16)
    outgoing = rounded[boundary]
    from_xlow = from_behind(outgoing[0], "px", 1)
    from_xhigh = from_behind(outgoing[1], "px", -1)
    from_ylow = from_behind(outgoing[2], "py", 1)
    from_yhigh = from_behind(outgoing[3], "py", -1)
    received = jnp.concatenate([from_xlow, from_xhigh, from_ylow, from_yhigh], axis=0)
    gathered = rounded[local_cols]
    product = jnp.einsum(
        "rtkj,rtij->rki", gathered, local_tiles, preferred_element_type=jnp.float32
    )
    coupled = jnp.einsum(
        "rkj,rij->rki", received[halo_slot], halo_tiles, preferred_element_type=jnp.float32
    )
    return product + coupled


def shards(start_vecs, local_tiles, local_cols, halo_tiles, halo_slot, boundary):

    def step_apply(current):
        return operator_apply(current, local_tiles, local_cols, halo_tiles, halo_slot, boundary)

    first_vecs = step_apply(start_vecs)

    def advance(step_index, state_pair):
        older_vec, newer_vec = state_pair
        return (newer_vec, 2.0 * step_apply(newer_vec) - older_vec)

    previous, current = lax.fori_loop(0, DEG - 1, advance, (start_vecs, first_vecs))
    total_rows = current.shape[0] * current.shape[2] * lax.axis_size("px") * lax.axis_size("py")
    partial_gram = jnp.einsum("rkj,rlj->kl", current, current, precision=lax.Precision.HIGHEST)
    raw_gram = butterfly_sum(butterfly_sum(partial_gram, "py"), "px")
    squares = jnp.diagonal(raw_gram)
    scales = lax.rsqrt(squares / total_rows + 1e-06)
    filtered = current * scales[None, :, None]
    gram_matrix = raw_gram * scales[:, None] * scales[None, :] / total_rows
    return (filtered, gram_matrix)


def solution(mesh):
    return jax.shard_map(
        shards,
        mesh=mesh,
        in_specs=(
            P(("px", "py"), None, None),
            P(("px", "py"), None, None, None),
            P(("px", "py"), None),
            P(("px", "py"), None, None),
            P(("px", "py")),
            P(("px", "py"), None),
        ),
        out_specs=(P(("px", "py"), None, None), P()),
        check_vma=False,
    )
```

```python
import jax
import jax.numpy as jnp
from jax import lax
from jax.sharding import PartitionSpec as P

DEG = 9


def from_behind(value, axis, steps):
    count = lax.axis_size(axis)
    pairs = [(source, (source + steps) % count) for source in range(count)]
    return lax.ppermute(value, axis, pairs)


def butterfly_sum(value, axis):
    count = lax.axis_size(axis)
    stride = 1
    while stride < count:
        pairs = [(source, source ^ stride) for source in range(count)]
        value = value + lax.ppermute(value, axis, pairs)
        stride *= 2
    return value


def exchange(outgoing, per_list):
    pieces = [outgoing[d * per_list:(d + 1) * per_list] for d in range(4)]
    from_xlow = from_behind(pieces[0], "px", 1)
    from_xhigh = from_behind(pieces[1], "px", -1)
    from_ylow = from_behind(pieces[2], "py", 1)
    from_yhigh = from_behind(pieces[3], "py", -1)
    return jnp.concatenate([from_xlow, from_xhigh, from_ylow, from_yhigh], axis=0)


def rows_apply(rounded, received, tiles, cols, halo, slot):
    gathered = rounded[cols]
    product = jnp.einsum(
        "rtkj,rtij->rki", gathered, tiles, preferred_element_type=jnp.float32
    )
    coupled = jnp.einsum(
        "rkj,rij->rki", received[slot], halo, preferred_element_type=jnp.float32
    )
    return product + coupled


def shards(start_vecs, local_tiles, local_cols, halo_tiles, halo_slot, boundary):
    per_list = boundary.shape[1]
    picks = boundary.reshape(-1)
    edge = (local_tiles[picks], local_cols[picks], halo_tiles[picks], halo_slot[picks])
    whole = (local_tiles, local_cols, halo_tiles, halo_slot)

    older = start_vecs
    rounded = start_vecs.astype(jnp.bfloat16)
    received = exchange(rounded[picks], per_list)
    edge_next = rows_apply(rounded, received, *edge)
    received_next = exchange(edge_next.astype(jnp.bfloat16), per_list)
    current = rows_apply(rounded, received, *whole)
    received = received_next
    for step in range(1, DEG):
        rounded = current.astype(jnp.bfloat16)
        if step < DEG - 1:
            edge_next = 2.0 * rows_apply(rounded, received, *edge) - older[picks]
            received_next = exchange(edge_next.astype(jnp.bfloat16), per_list)
        newer = 2.0 * rows_apply(rounded, received, *whole) - older
        older, current = current, newer
        if step < DEG - 1:
            received = received_next

    total_rows = current.shape[0] * current.shape[2] * lax.axis_size("px") * lax.axis_size("py")
    partial_gram = jnp.einsum("rkj,rlj->kl", current, current, precision=lax.Precision.HIGHEST)
    raw_gram = butterfly_sum(butterfly_sum(partial_gram, "py"), "px")
    squares = jnp.diagonal(raw_gram)
    scales = lax.rsqrt(squares / total_rows + 1e-06)
    filtered = current * scales[None, :, None]
    gram_matrix = raw_gram * scales[:, None] * scales[None, :] / total_rows
    return (filtered, gram_matrix)


def solution(mesh):
    return jax.shard_map(
        shards,
        mesh=mesh,
        in_specs=(
            P(("px", "py"), None, None),
            P(("px", "py"), None, None, None),
            P(("px", "py"), None),
            P(("px", "py"), None, None),
            P(("px", "py")),
            P(("px", "py"), None),
        ),
        out_specs=(P(("px", "py"), None, None), P()),
        check_vma=False,
    )
```

```python
import jax
import jax.numpy as jnp
from jax import lax
from jax.sharding import PartitionSpec as P

DEG = 9


def from_behind(value, axis, steps):
    count = lax.axis_size(axis)
    pairs = [(source, (source + steps) % count) for source in range(count)]
    return lax.ppermute(value, axis, pairs)


def butterfly_sum(value, axis):
    count = lax.axis_size(axis)
    stride = 1
    while stride < count:
        pairs = [(source, source ^ stride) for source in range(count)]
        value = value + lax.ppermute(value, axis, pairs)
        stride *= 2
    return value


def exchange(outgoing, per_list):
    pieces = [outgoing[d * per_list:(d + 1) * per_list] for d in range(4)]
    return [
        from_behind(pieces[0], "px", 1),
        from_behind(pieces[1], "px", -1),
        from_behind(pieces[2], "py", 1),
        from_behind(pieces[3], "py", -1),
    ]


def halo_term(pieces, chooser, halo):
    received = jnp.concatenate(pieces, axis=0)
    chosen = jnp.einsum("rs,skj->rkj", chooser, received, preferred_element_type=jnp.float32)
    return jnp.einsum(
        "rkj,rij->rki", chosen.astype(jnp.bfloat16), halo, preferred_element_type=jnp.float32
    )


def local_term(rounded, tiles, cols):
    return jnp.einsum(
        "rtkj,rtij->rki", rounded[cols], tiles, preferred_element_type=jnp.float32
    )


def shards(start_vecs, local_tiles, local_cols, halo_tiles, halo_slot, boundary):
    per_list = boundary.shape[1]
    slots = 4 * per_list
    picks = boundary.reshape(-1)
    edge_halo = halo_tiles[picks]
    edge_chooser = jax.nn.one_hot(halo_slot[picks], slots, dtype=jnp.bfloat16)
    whole_chooser = jax.nn.one_hot(halo_slot, slots, dtype=jnp.bfloat16)

    rounded = start_vecs.astype(jnp.bfloat16)
    received = exchange(rounded[picks], per_list)
    local_part = local_term(rounded, local_tiles, local_cols)
    edge_next = local_part[picks] + halo_term(received, edge_chooser, edge_halo)
    received_next = exchange(edge_next.astype(jnp.bfloat16), per_list)
    older = start_vecs
    current = local_part + halo_term(received, whole_chooser, halo_tiles)
    received = received_next
    for step in range(1, DEG):
        rounded = current.astype(jnp.bfloat16)
        local_part = 2.0 * local_term(rounded, local_tiles, local_cols) - older
        if step < DEG - 1:
            edge_next = local_part[picks] + 2.0 * halo_term(received, edge_chooser, edge_halo)
            received_next = exchange(edge_next.astype(jnp.bfloat16), per_list)
        newer = local_part + 2.0 * halo_term(received, whole_chooser, halo_tiles)
        older, current = current, newer
        if step < DEG - 1:
            received = received_next

    total_rows = current.shape[0] * current.shape[2] * lax.axis_size("px") * lax.axis_size("py")
    partial_gram = jnp.einsum("rkj,rlj->kl", current, current, precision=lax.Precision.HIGHEST)
    raw_gram = butterfly_sum(butterfly_sum(partial_gram, "py"), "px")
    squares = jnp.diagonal(raw_gram)
    scales = lax.rsqrt(squares / total_rows + 1e-06)
    filtered = current * scales[None, :, None]
    gram_matrix = raw_gram * scales[:, None] * scales[None, :] / total_rows
    return (filtered, gram_matrix)


def solution(mesh):
    return jax.shard_map(
        shards,
        mesh=mesh,
        in_specs=(
            P(("px", "py"), None, None),
            P(("px", "py"), None, None, None),
            P(("px", "py"), None),
            P(("px", "py"), None, None),
            P(("px", "py")),
            P(("px", "py"), None),
        ),
        out_specs=(P(("px", "py"), None, None), P()),
        check_vma=False,
    )
```

```python
import jax
import jax.numpy as jnp
from jax import lax
from jax.sharding import PartitionSpec as P


DEG = 9


def from_behind(value, axis, steps):
    count = lax.axis_size(axis)
    pairs = [(source, (source + steps) % count) for source in range(count)]
    return lax.ppermute(value, axis, pairs)


def butterfly_sum(value, axis):
    count = lax.axis_size(axis)
    stride = 1
    while stride < count:
        pairs = [(source, source ^ stride) for source in range(count)]
        value = value + lax.ppermute(value, axis, pairs)
        stride *= 2
    return value


def exchange(outgoing, per_list, fillers=()):
    pieces = [outgoing[d * per_list:(d + 1) * per_list] for d in range(4)]
    routes = [("px", 1), ("px", -1), ("py", 1), ("py", -1)]
    received = []
    carried = None
    for d, (axis, steps) in enumerate(routes):
        piece = pieces[d]
        if d > 0 and d - 1 < len(fillers):
            carried = fillers[d - 1](carried)
            piece, carried = lax.optimization_barrier((piece, carried))
        received.append(from_behind(piece, axis, steps))
    for filler in fillers[3:]:
        carried = filler(carried)
    return received, carried


def halo_term(pieces, chooser, halo):
    received = jnp.concatenate(pieces, axis=0)
    chosen = jnp.einsum("rs,skj->rkj", chooser, received, preferred_element_type=jnp.float32)
    return jnp.einsum(
        "rkj,rij->rki", chosen.astype(jnp.bfloat16), halo, preferred_element_type=jnp.float32
    )


def local_term(rounded, tiles, cols):
    return jnp.einsum(
        "rtkj,rtij->rki", rounded[cols], tiles, preferred_element_type=jnp.float32
    )


def shards(start_vecs, local_tiles, local_cols, halo_tiles, halo_slot, boundary):
    per_list = boundary.shape[1]
    slots = 4 * per_list
    picks = boundary.reshape(-1)
    edge_halo = halo_tiles[picks]
    edge_chooser = jax.nn.one_hot(halo_slot[picks], slots, dtype=jnp.bfloat16)
    whole_chooser = jax.nn.one_hot(halo_slot, slots, dtype=jnp.bfloat16)

    rounded = start_vecs.astype(jnp.bfloat16)
    received, _ = exchange(rounded[picks], per_list)
    local_part = local_term(rounded, local_tiles, local_cols)
    edge_next = local_part[picks] + halo_term(received, edge_chooser, edge_halo)
    older = start_vecs
    for step in range(1, DEG):
      halo_scale = 1.0 if step == 1 else 2.0
      state = (older, local_part, received)

      def whole_vector(carried, state=state, halo_scale=halo_scale):
          _, local_vec, blocks = state
          return local_vec + halo_scale * halo_term(blocks, whole_chooser, halo_tiles)

      def gathered_blocks(carried):
          return carried, carried.astype(jnp.bfloat16)[local_cols]

      def next_local(carried, older_vec=older):
          current_vec, gathered = carried
          product = jnp.einsum(
              "rtkj,rtij->rki", gathered, local_tiles, preferred_element_type=jnp.float32
          )
          return current_vec, 2.0 * product - older_vec

      def next_edge(carried):
          current_vec, local_vec = carried
          return current_vec, local_vec, local_vec[picks]

      received_next, (current, local_part, edge_local) = exchange(
          edge_next.astype(jnp.bfloat16), per_list,
          (whole_vector, gathered_blocks, next_local, next_edge),
      )
      older = current
      received = received_next
      edge_next = edge_local + 2.0 * halo_term(received, edge_chooser, edge_halo)
    current = local_part + 2.0 * halo_term(received, whole_chooser, halo_tiles)

    total_rows = current.shape[0] * current.shape[2] * lax.axis_size("px") * lax.axis_size("py")
    partial_gram = jnp.einsum("rkj,rlj->kl", current, current, precision=lax.Precision.HIGHEST)
    raw_gram = butterfly_sum(butterfly_sum(partial_gram, "py"), "px")
    squares = jnp.diagonal(raw_gram)
    scales = lax.rsqrt(squares / total_rows + 1e-06)
    filtered = current * scales[None, :, None]
    gram_matrix = raw_gram * scales[:, None] * scales[None, :] / total_rows
    return (filtered, gram_matrix)


def solution(mesh):
    return jax.shard_map(
        shards,
        mesh=mesh,
        in_specs=(
            P(("px", "py"), None, None),
            P(("px", "py"), None, None, None),
            P(("px", "py"), None),
            P(("px", "py"), None, None),
            P(("px", "py")),
            P(("px", "py"), None),
        ),
        out_specs=(P(("px", "py"), None, None), P()),
        check_vma=False,
    )
```

```python
import functools

import jax
import jax.numpy as jnp
from jax import lax
from jax.experimental import pallas as pl
from jax.experimental.pallas import tpu as pltpu
from jax.sharding import PartitionSpec as P

DEG = 9
INTERPRET = False
CONTRACT_LAST = (((1,), (1,)), ((), ()))


def from_behind(value, axis, steps):
    count = lax.axis_size(axis)
    pairs = [(source, (source + steps) % count) for source in range(count)]
    return lax.ppermute(value, axis, pairs)


def butterfly_sum(value, axis):
    count = lax.axis_size(axis)
    stride = 1
    while stride < count:
        pairs = [(source, source ^ stride) for source in range(count)]
        value = value + lax.ppermute(value, axis, pairs)
        stride *= 2
    return value


def _local_kernel(cols_ref, rounded_ref, tiles_ref, out_ref):
    rows, per_row = tiles_ref.shape[0], tiles_ref.shape[1]
    for r in range(rows):
        acc = None
        for t in range(per_row):
            block = rounded_ref[cols_ref[r * per_row + t]]
            part = lax.dot_general(
                block, tiles_ref[r, t], CONTRACT_LAST, preferred_element_type=jnp.float32
            )
            acc = part if acc is None else acc + part
        out_ref[r] = acc


def local_product(rounded, tiles, cols):
    vmem = pl.BlockSpec(memory_space=pltpu.VMEM)
    return pl.pallas_call(
        _local_kernel,
        out_shape=jax.ShapeDtypeStruct((tiles.shape[0],) + rounded.shape[1:], jnp.float32),
        in_specs=[pl.BlockSpec(memory_space=pltpu.SMEM), vmem, vmem],
        out_specs=vmem,
        interpret=INTERPRET,
    )(cols.reshape(-1), rounded, tiles)


def _combine_kernel(slot_ref, picks_ref, local_ref, older_ref, halo_ref, *refs, scale, with_older):
    pieces, (vec_ref, rounded_ref), edge_refs, (received_ref,) = refs[:4], refs[4:6], refs[6:10], refs[10:]
    per_list = pieces[0].shape[0]
    for d in range(4):
        for i in range(per_list):
            received_ref[d * per_list + i] = pieces[d][i]
    for r in range(local_ref.shape[0]):
        block = received_ref[slot_ref[r]]
        coupled = lax.dot_general(
            block, halo_ref[r], CONTRACT_LAST, preferred_element_type=jnp.float32
        )
        value = local_ref[r] + coupled
        if with_older:
            value = scale * value - older_ref[r]
        vec_ref[r] = value
        rounded_ref[r] = value.astype(jnp.bfloat16)
    for d in range(4):
        for i in range(per_list):
            edge_refs[d][i] = rounded_ref[picks_ref[d * per_list + i]]


def combine(local, older, pieces, halo, slot, picks, scale, with_older):
    vmem = pl.BlockSpec(memory_space=pltpu.VMEM)
    smem = pl.BlockSpec(memory_space=pltpu.SMEM)
    per_list = pieces[0].shape[0]
    piece_shape = jax.ShapeDtypeStruct(pieces[0].shape, jnp.bfloat16)
    kernel = functools.partial(_combine_kernel, scale=scale, with_older=with_older)
    outs = pl.pallas_call(
        kernel,
        out_shape=(
            jax.ShapeDtypeStruct(local.shape, jnp.float32),
            jax.ShapeDtypeStruct(local.shape, jnp.bfloat16),
        ) + (piece_shape,) * 4,
        in_specs=[smem, smem] + [vmem] * 7,
        out_specs=(vmem,) * 6,
        scratch_shapes=[pltpu.VMEM((4 * per_list,) + pieces[0].shape[1:], jnp.bfloat16)],
        interpret=INTERPRET,
    )(slot, picks, local, older, halo, *pieces)
    return outs[0], outs[1], list(outs[2:])


def exchange(pieces):
    return [
        from_behind(pieces[0], "px", 1),
        from_behind(pieces[1], "px", -1),
        from_behind(pieces[2], "py", 1),
        from_behind(pieces[3], "py", -1),
    ]


def shards(start_vecs, local_tiles, local_cols, halo_tiles, halo_slot, boundary):
    per_list = boundary.shape[1]
    picks = boundary.reshape(-1)
    rounded = start_vecs.astype(jnp.bfloat16)
    outgoing = [rounded[boundary[d]] for d in range(4)]
    older = start_vecs
    current = start_vecs
    for step in range(DEG):
        received = exchange(outgoing)
        local = local_product(rounded, local_tiles, local_cols)
        newer, rounded, outgoing = combine(
            local, older, received, halo_tiles, halo_slot, picks, 2.0, step > 0
        )
        older, current = current, newer

    total_rows = current.shape[0] * current.shape[2] * lax.axis_size("px") * lax.axis_size("py")
    partial_gram = jnp.einsum("rkj,rlj->kl", current, current, precision=lax.Precision.HIGHEST)
    raw_gram = butterfly_sum(butterfly_sum(partial_gram, "py"), "px")
    squares = jnp.diagonal(raw_gram)
    scales = lax.rsqrt(squares / total_rows + 1e-06)
    filtered = current * scales[None, :, None]
    gram_matrix = raw_gram * scales[:, None] * scales[None, :] / total_rows
    return (filtered, gram_matrix)


def solution(mesh):
    return jax.shard_map(
        shards,
        mesh=mesh,
        in_specs=(
            P(("px", "py"), None, None),
            P(("px", "py"), None, None, None),
            P(("px", "py"), None),
            P(("px", "py"), None, None),
            P(("px", "py")),
            P(("px", "py"), None),
        ),
        out_specs=(P(("px", "py"), None, None), P()),
        check_vma=False,
    )
```

```python
import functools

import jax
import jax.numpy as jnp
from jax import lax
from jax.experimental import pallas as pl
from jax.experimental.pallas import tpu as pltpu
from jax.sharding import PartitionSpec as P


DEG = 9
INTERPRET = False


def from_behind(value, axis, steps):
    count = lax.axis_size(axis)
    pairs = [(source, (source + steps) % count) for source in range(count)]
    return lax.ppermute(value, axis, pairs)


def butterfly_sum(value, axis):
    count = lax.axis_size(axis)
    stride = 1
    while stride < count:
        pairs = [(source, source ^ stride) for source in range(count)]
        value = value + lax.ppermute(value, axis, pairs)
        stride *= 2
    return value


def _local_kernel(cols_ref, rounded_ref, stacked_ref, out_ref):
    rows = stacked_ref.shape[0]
    per_row = stacked_ref.shape[1] // rounded_ref.shape[2]
    for r in range(rows):
        blocks = [rounded_ref[cols_ref[r * per_row + t]] for t in range(per_row)]
        out_ref[r] = jnp.dot(
            jnp.concatenate(blocks, axis=1), stacked_ref[r], preferred_element_type=jnp.float32
        )


def local_product(rounded, stacked, cols):
    vmem = pl.BlockSpec(memory_space=pltpu.VMEM)
    return pl.pallas_call(
        _local_kernel,
        out_shape=jax.ShapeDtypeStruct((stacked.shape[0],) + rounded.shape[1:], jnp.float32),
        in_specs=[pl.BlockSpec(memory_space=pltpu.SMEM), vmem, vmem],
        out_specs=vmem,
        interpret=INTERPRET,
    )(cols.reshape(-1), rounded, stacked)


def _combine_kernel(slot_ref, picks_ref, local_ref, older_ref, halo_ref, *refs, scale, with_older):
    pieces, (vec_ref, rounded_ref), edge_refs, (received_ref,) = refs[:4], refs[4:6], refs[6:10], refs[10:]
    per_list = pieces[0].shape[0]
    for d in range(4):
        for i in range(per_list):
            received_ref[d * per_list + i] = pieces[d][i]
    for r in range(local_ref.shape[0]):
        block = received_ref[slot_ref[r]]
        coupled = jnp.dot(block, halo_ref[r], preferred_element_type=jnp.float32)
        value = local_ref[r] + coupled
        if with_older:
            value = scale * value - older_ref[r]
        vec_ref[r] = value
        rounded_ref[r] = value.astype(jnp.bfloat16)
    for d in range(4):
        for i in range(per_list):
            edge_refs[d][i] = rounded_ref[picks_ref[d * per_list + i]]


def combine(local, older, pieces, halo, slot, picks, scale, with_older):
    vmem = pl.BlockSpec(memory_space=pltpu.VMEM)
    smem = pl.BlockSpec(memory_space=pltpu.SMEM)
    per_list = pieces[0].shape[0]
    piece_shape = jax.ShapeDtypeStruct(pieces[0].shape, jnp.bfloat16)
    kernel = functools.partial(_combine_kernel, scale=scale, with_older=with_older)
    outs = pl.pallas_call(
        kernel,
        out_shape=(
            jax.ShapeDtypeStruct(local.shape, jnp.float32),
            jax.ShapeDtypeStruct(local.shape, jnp.bfloat16),
        ) + (piece_shape,) * 4,
        in_specs=[smem, smem] + [vmem] * 7,
        out_specs=(vmem,) * 6,
        scratch_shapes=[pltpu.VMEM((4 * per_list,) + pieces[0].shape[1:], jnp.bfloat16)],
        interpret=INTERPRET,
    )(slot, picks, local, older, halo, *pieces)
    return outs[0], outs[1], list(outs[2:])


def exchange(pieces):
    from_yhigh = from_behind(pieces[3], "py", -1)
    from_ylow = from_behind(pieces[2], "py", 1)
    from_xhigh = from_behind(pieces[1], "px", -1)
    from_xlow = from_behind(pieces[0], "px", 1)
    return [from_xlow, from_xhigh, from_ylow, from_yhigh]


def shards(start_vecs, local_tiles, local_cols, halo_tiles, halo_slot, boundary):
    picks = boundary.reshape(-1)
    rounded = start_vecs.astype(jnp.bfloat16)
    outgoing = [rounded[boundary[d]] for d in range(4)]
    rows, per_row, size = local_tiles.shape[0], local_tiles.shape[1], local_tiles.shape[3]
    stacked = jnp.swapaxes(local_tiles, 2, 3).reshape(rows, per_row * size, size)
    halo_t = jnp.swapaxes(halo_tiles, 1, 2)
    older = start_vecs
    current = start_vecs
    for step in range(DEG):
        received = exchange(outgoing)
        local = local_product(rounded, stacked, local_cols)
        newer, rounded, outgoing = combine(
            local, older, received, halo_t, halo_slot, picks, 2.0, step > 0
        )
        older, current = current, newer

    total_rows = current.shape[0] * current.shape[2] * lax.axis_size("px") * lax.axis_size("py")
    partial_gram = jnp.einsum("rkj,rlj->kl", current, current, precision=lax.Precision.HIGHEST)
    raw_gram = butterfly_sum(butterfly_sum(partial_gram, "py"), "px")
    squares = jnp.diagonal(raw_gram)
    scales = lax.rsqrt(squares / total_rows + 1e-06)
    filtered = current * scales[None, :, None]
    gram_matrix = raw_gram * scales[:, None] * scales[None, :] / total_rows
    return (filtered, gram_matrix)


def solution(mesh):
    return jax.shard_map(
        shards,
        mesh=mesh,
        in_specs=(
            P(("px", "py"), None, None),
            P(("px", "py"), None, None, None),
            P(("px", "py"), None),
            P(("px", "py"), None, None),
            P(("px", "py")),
            P(("px", "py"), None),
        ),
        out_specs=(P(("px", "py"), None, None), P()),
        check_vma=False,
    )
```

```python
import functools

import jax
import jax.numpy as jnp
from jax import lax
from jax.experimental import pallas as pl
from jax.experimental.pallas import tpu as pltpu
from jax.sharding import PartitionSpec as P


DEG = 9
INTERPRET = False


def from_behind(value, axis, steps):
    count = lax.axis_size(axis)
    pairs = [(source, (source + steps) % count) for source in range(count)]
    return lax.ppermute(value, axis, pairs)


def butterfly_sum(value, axis):
    count = lax.axis_size(axis)
    stride = 1
    while stride < count:
        pairs = [(source, source ^ stride) for source in range(count)]
        value = value + lax.ppermute(value, axis, pairs)
        stride *= 2
    return value


def _local_kernel(cols_ref, picks_ref, rounded_ref, stacked_ref, *refs, scale, with_older):
    if with_older:
        older_ref, part_ref, edge_ref = refs
    else:
        part_ref, edge_ref = refs
    rows = stacked_ref.shape[0]
    per_row = stacked_ref.shape[1] // rounded_ref.shape[2]
    for r in range(rows):
        blocks = [rounded_ref[cols_ref[r * per_row + t]] for t in range(per_row)]
        value = jnp.dot(
            jnp.concatenate(blocks, axis=1), stacked_ref[r], preferred_element_type=jnp.float32
        )
        if with_older:
            value = scale * value - older_ref[r]
        part_ref[r] = value
    for e in range(edge_ref.shape[0]):
        edge_ref[e] = part_ref[picks_ref[e]]


def local_part(rounded, stacked, cols, picks, older, scale):
    vmem = pl.BlockSpec(memory_space=pltpu.VMEM)
    smem = pl.BlockSpec(memory_space=pltpu.SMEM)
    with_older = older is not None
    shape = (stacked.shape[0],) + rounded.shape[1:]
    kernel = functools.partial(_local_kernel, scale=scale, with_older=with_older)
    operands = (cols.reshape(-1), picks, rounded, stacked) + ((older,) if with_older else ())
    return pl.pallas_call(
        kernel,
        out_shape=(
            jax.ShapeDtypeStruct(shape, jnp.float32),
            jax.ShapeDtypeStruct((picks.shape[0],) + shape[1:], jnp.float32),
        ),
        in_specs=[smem, smem] + [vmem] * (len(operands) - 2),
        out_specs=(vmem, vmem),
        interpret=INTERPRET,
    )(*operands)


def _halo_kernel(slot_ref, part_ref, halo_ref, *refs, scale, rounded_only):
    pieces, outs, received_ref = refs[:4], refs[4:-1], refs[-1]
    per_list = pieces[0].shape[0]
    for d in range(4):
        for i in range(per_list):
            received_ref[d * per_list + i] = pieces[d][i]
    for r in range(part_ref.shape[0]):
        block = received_ref[slot_ref[r]]
        coupled = jnp.dot(block, halo_ref[r], preferred_element_type=jnp.float32)
        value = part_ref[r] + (coupled if scale == 1.0 else scale * coupled)
        if rounded_only:
            outs[r // per_list][r % per_list] = value.astype(jnp.bfloat16)
        else:
            outs[0][r] = value
            outs[1][r] = value.astype(jnp.bfloat16)


def halo_add(part, pieces, halo, slot, scale, rounded_only):
    vmem = pl.BlockSpec(memory_space=pltpu.VMEM)
    smem = pl.BlockSpec(memory_space=pltpu.SMEM)
    per_list = pieces[0].shape[0]
    if rounded_only:
        out_shape = (jax.ShapeDtypeStruct(pieces[0].shape, jnp.bfloat16),) * 4
    else:
        out_shape = (
            jax.ShapeDtypeStruct(part.shape, jnp.float32),
            jax.ShapeDtypeStruct(part.shape, jnp.bfloat16),
        )
    kernel = functools.partial(_halo_kernel, scale=scale, rounded_only=rounded_only)
    outs = pl.pallas_call(
        kernel,
        out_shape=out_shape,
        in_specs=[smem] + [vmem] * 6,
        out_specs=(vmem,) * len(out_shape),
        scratch_shapes=[pltpu.VMEM((4 * per_list,) + pieces[0].shape[1:], jnp.bfloat16)],
        interpret=INTERPRET,
    )(slot, part, halo, *pieces)
    return list(outs)


def exchange(pieces):
    from_yhigh = from_behind(pieces[3], "py", -1)
    from_ylow = from_behind(pieces[2], "py", 1)
    from_xhigh = from_behind(pieces[1], "px", -1)
    from_xlow = from_behind(pieces[0], "px", 1)
    return [from_xlow, from_xhigh, from_ylow, from_yhigh]


def shards(start_vecs, local_tiles, local_cols, halo_tiles, halo_slot, boundary):
    picks = boundary.reshape(-1)
    rounded = start_vecs.astype(jnp.bfloat16)
    outgoing = [rounded[boundary[d]] for d in range(4)]
    rows, per_row, size = local_tiles.shape[0], local_tiles.shape[1], local_tiles.shape[3]
    stacked = jnp.swapaxes(local_tiles, 2, 3).reshape(rows, per_row * size, size)
    halo_t = jnp.swapaxes(halo_tiles, 1, 2)
    edge_halo = halo_t[picks]
    edge_slot = halo_slot[picks]
    outgoing = [rounded[boundary[d]] for d in range(4)]
    received = exchange(outgoing)
    part, edge_part = local_part(rounded, stacked, local_cols, picks, None, 1.0)
    previous = start_vecs
    for step in range(1, DEG + 1):
        scale = 1.0 if step == 1 else 2.0
        if step < DEG:
            outgoing = halo_add(edge_part, received, edge_halo, edge_slot, scale, True)
            received_next = exchange(outgoing)
        current, rounded = halo_add(part, received, halo_t, halo_slot, scale, False)
        if step < DEG:
            part, edge_part = local_part(rounded, stacked, local_cols, picks, previous, 2.0)
        if step < DEG:
            received = received_next
        previous = current

    total_rows = current.shape[0] * current.shape[2] * lax.axis_size("px") * lax.axis_size("py")
    partial_gram = jnp.einsum("rkj,rlj->kl", current, current, precision=lax.Precision.HIGHEST)
    raw_gram = butterfly_sum(butterfly_sum(partial_gram, "py"), "px")
    squares = jnp.diagonal(raw_gram)
    scales = lax.rsqrt(squares / total_rows + 1e-06)
    filtered = current * scales[None, :, None]
    gram_matrix = raw_gram * scales[:, None] * scales[None, :] / total_rows
    return (filtered, gram_matrix)


def solution(mesh):
    return jax.shard_map(
        shards,
        mesh=mesh,
        in_specs=(
            P(("px", "py"), None, None),
            P(("px", "py"), None, None, None),
            P(("px", "py"), None),
            P(("px", "py"), None, None),
            P(("px", "py")),
            P(("px", "py"), None),
        ),
        out_specs=(P(("px", "py"), None, None), P()),
        check_vma=False,
    )
```

```python
import jax
import jax.numpy as jnp
from jax import lax
from jax.sharding import PartitionSpec as P

DEG = 9


def from_behind(value, axis, steps):
    count = lax.axis_size(axis)
    pairs = [(source, (source + steps) % count) for source in range(count)]
    return lax.ppermute(value, axis, pairs)


def butterfly_sum(value, axis):
    count = lax.axis_size(axis)
    stride = 1
    while stride < count:
        pairs = [(source, source ^ stride) for source in range(count)]
        value = value + lax.ppermute(value, axis, pairs)
        stride *= 2
    return value


def operator_apply(current, local_tiles, local_cols, halo_tiles, halo_slot, boundary):
    rounded = current.astype(jnp.bfloat16)
    outgoing = rounded[boundary]
    from_xlow = from_behind(outgoing[0], "px", 1)
    from_xhigh = from_behind(outgoing[1], "px", -1)
    from_ylow = from_behind(outgoing[2], "py", 1)
    from_yhigh = from_behind(outgoing[3], "py", -1)
    received = jnp.concatenate([from_xlow, from_xhigh, from_ylow, from_yhigh], axis=0)
    gathered = rounded[local_cols]
    product = jnp.einsum(
        "rtkj,rtij->rki", gathered, local_tiles, preferred_element_type=jnp.float32
    )
    coupled = jnp.einsum(
        "rkj,rij->rki", received[halo_slot], halo_tiles, preferred_element_type=jnp.float32
    )
    return product + coupled


def shards(start_vecs, local_tiles, local_cols, halo_tiles, halo_slot, boundary):

    def step_apply(current):
        return operator_apply(current, local_tiles, local_cols, halo_tiles, halo_slot, boundary)

    first_vecs = step_apply(start_vecs)

    previous, current = start_vecs, first_vecs
    for step_index in range(DEG - 1):
        previous, current = current, 2.0 * step_apply(current) - previous
    total_rows = current.shape[0] * current.shape[2] * lax.axis_size("px") * lax.axis_size("py")
    partial_gram = jnp.einsum("rkj,rlj->kl", current, current, precision=lax.Precision.HIGHEST)
    raw_gram = butterfly_sum(butterfly_sum(partial_gram, "py"), "px")
    squares = jnp.diagonal(raw_gram)
    scales = lax.rsqrt(squares / total_rows + 1e-06)
    filtered = current * scales[None, :, None]
    gram_matrix = raw_gram * scales[:, None] * scales[None, :] / total_rows
    return (filtered, gram_matrix)


def solution(mesh):
    return jax.shard_map(
        shards,
        mesh=mesh,
        in_specs=(
            P(("px", "py"), None, None),
            P(("px", "py"), None, None, None),
            P(("px", "py"), None),
            P(("px", "py"), None, None),
            P(("px", "py")),
            P(("px", "py"), None),
        ),
        out_specs=(P(("px", "py"), None, None), P()),
        check_vma=False,
    )
```

```python
import jax
import jax.numpy as jnp
from jax import lax
from jax.sharding import PartitionSpec as P

DEG = 9


def from_behind(value, axis, steps):
    count = lax.axis_size(axis)
    pairs = [(source, (source + steps) % count) for source in range(count)]
    return lax.ppermute(value, axis, pairs)


def gathered_sum(value, axis):
    return jnp.sum(lax.all_gather(value, axis), axis=0)


def operator_apply(current, local_tiles, local_cols, halo_tiles, halo_slot, boundary):
    rounded = current.astype(jnp.bfloat16)
    outgoing = rounded[boundary]
    from_xlow = from_behind(outgoing[0], "px", 1)
    from_xhigh = from_behind(outgoing[1], "px", -1)
    from_ylow = from_behind(outgoing[2], "py", 1)
    from_yhigh = from_behind(outgoing[3], "py", -1)
    received = jnp.concatenate([from_xlow, from_xhigh, from_ylow, from_yhigh], axis=0)
    gathered = rounded[local_cols]
    product = jnp.einsum(
        "rtkj,rtij->rki", gathered, local_tiles, preferred_element_type=jnp.float32
    )
    coupled = jnp.einsum(
        "rkj,rij->rki", received[halo_slot], halo_tiles, preferred_element_type=jnp.float32
    )
    return product + coupled


def shards(start_vecs, local_tiles, local_cols, halo_tiles, halo_slot, boundary):

    def step_apply(current):
        return operator_apply(current, local_tiles, local_cols, halo_tiles, halo_slot, boundary)

    first_vecs = step_apply(start_vecs)

    def advance(step_index, state_pair):
        older_vec, newer_vec = state_pair
        return (newer_vec, 2.0 * step_apply(newer_vec) - older_vec)

    previous, current = lax.fori_loop(0, DEG - 1, advance, (start_vecs, first_vecs))
    total_rows = current.shape[0] * current.shape[2] * lax.axis_size("px") * lax.axis_size("py")
    partial_gram = jnp.einsum("rkj,rlj->kl", current, current, precision=lax.Precision.HIGHEST)
    raw_gram = gathered_sum(gathered_sum(partial_gram, "py"), "px")
    squares = jnp.diagonal(raw_gram)
    scales = lax.rsqrt(squares / total_rows + 1e-06)
    filtered = current * scales[None, :, None]
    gram_matrix = raw_gram * scales[:, None] * scales[None, :] / total_rows
    return (filtered, gram_matrix)


def solution(mesh):
    return jax.shard_map(
        shards,
        mesh=mesh,
        in_specs=(
            P(("px", "py"), None, None),
            P(("px", "py"), None, None, None),
            P(("px", "py"), None),
            P(("px", "py"), None, None),
            P(("px", "py")),
            P(("px", "py"), None),
        ),
        out_specs=(P(("px", "py"), None, None), P()),
        check_vma=False,
    )
```

```python
import jax
import jax.numpy as jnp
from jax import lax
from jax.sharding import PartitionSpec as P

DEG = 9


def from_behind(value, axis, steps):
    count = lax.axis_size(axis)
    pairs = [(source, (source + steps) % count) for source in range(count)]
    return lax.ppermute(value, axis, pairs)


def gathered_sum(value, axis):
    return jnp.sum(lax.all_gather(value, axis), axis=0)


def fold_symmetric(gram):
    half = gram.shape[0] // 2
    top, side, low = gram[:half, :half], gram[:half, half:], gram[half:, half:]
    upper = jnp.arange(half)[:, None] <= jnp.arange(half)[None, :]
    mixed = jnp.where(upper, top, low)
    return jnp.concatenate([side, mixed, jnp.diagonal(low)[None, :]], axis=0)


def unfold_symmetric(folded):
    half = folded.shape[1]
    side, mixed, low_diag = folded[:half], folded[half:2 * half], folded[2 * half]
    rows, cols = jnp.arange(half)[:, None], jnp.arange(half)[None, :]
    top = jnp.where(rows <= cols, mixed, mixed.T)
    low = jnp.where(rows > cols, mixed, mixed.T)
    low = jnp.where(rows == cols, low_diag[None, :], low)
    return jnp.concatenate(
        [jnp.concatenate([top, side], axis=1), jnp.concatenate([side.T, low], axis=1)], axis=0
    )


def operator_apply(current, local_tiles, local_cols, halo_tiles, halo_slot, boundary):
    rounded = current.astype(jnp.bfloat16)
    outgoing = rounded[boundary]
    from_xlow = from_behind(outgoing[0], "px", 1)
    from_xhigh = from_behind(outgoing[1], "px", -1)
    from_ylow = from_behind(outgoing[2], "py", 1)
    from_yhigh = from_behind(outgoing[3], "py", -1)
    received = jnp.concatenate([from_xlow, from_xhigh, from_ylow, from_yhigh], axis=0)
    gathered = rounded[local_cols]
    product = jnp.einsum(
        "rtkj,rtij->rki", gathered, local_tiles, preferred_element_type=jnp.float32
    )
    coupled = jnp.einsum(
        "rkj,rij->rki", received[halo_slot], halo_tiles, preferred_element_type=jnp.float32
    )
    return product + coupled


def shards(start_vecs, local_tiles, local_cols, halo_tiles, halo_slot, boundary):

    def step_apply(current):
        return operator_apply(current, local_tiles, local_cols, halo_tiles, halo_slot, boundary)

    first_vecs = step_apply(start_vecs)

    def advance(step_index, state_pair):
        older_vec, newer_vec = state_pair
        return (newer_vec, 2.0 * step_apply(newer_vec) - older_vec)

    previous, current = lax.fori_loop(0, DEG - 1, advance, (start_vecs, first_vecs))
    total_rows = current.shape[0] * current.shape[2] * lax.axis_size("px") * lax.axis_size("py")
    partial_gram = jnp.einsum("rkj,rlj->kl", current, current, precision=lax.Precision.HIGHEST)
    raw_gram = unfold_symmetric(gathered_sum(gathered_sum(fold_symmetric(partial_gram), "py"), "px"))
    squares = jnp.diagonal(raw_gram)
    scales = lax.rsqrt(squares / total_rows + 1e-06)
    filtered = current * scales[None, :, None]
    gram_matrix = raw_gram * scales[:, None] * scales[None, :] / total_rows
    return (filtered, gram_matrix)


def solution(mesh):
    return jax.shard_map(
        shards,
        mesh=mesh,
        in_specs=(
            P(("px", "py"), None, None),
            P(("px", "py"), None, None, None),
            P(("px", "py"), None),
            P(("px", "py"), None, None),
            P(("px", "py")),
            P(("px", "py"), None),
        ),
        out_specs=(P(("px", "py"), None, None), P()),
        check_vma=False,
    )
```

```python
import jax
import jax.numpy as jnp
from jax import lax
from jax.sharding import PartitionSpec as P

DEG = 9


def from_behind(value, axis, steps):
    count = lax.axis_size(axis)
    pairs = [(source, (source + steps) % count) for source in range(count)]
    return lax.ppermute(value, axis, pairs)


def gathered_sum(value, axis):
    return jnp.sum(lax.all_gather(value, axis), axis=0)


def fold_symmetric(gram):
    half = gram.shape[0] // 2
    top, side, low = gram[:half, :half], gram[:half, half:], gram[half:, half:]
    upper = jnp.arange(half)[:, None] <= jnp.arange(half)[None, :]
    mixed = jnp.where(upper, top, low)
    return jnp.concatenate([side, mixed, jnp.diagonal(low)[None, :]], axis=0)


def unfold_symmetric(folded):
    half = folded.shape[1]
    side, mixed, low_diag = folded[:half], folded[half:2 * half], folded[2 * half]
    rows, cols = jnp.arange(half)[:, None], jnp.arange(half)[None, :]
    top = jnp.where(rows <= cols, mixed, mixed.T)
    low = jnp.where(rows > cols, mixed, mixed.T)
    low = jnp.where(rows == cols, low_diag[None, :], low)
    return jnp.concatenate(
        [jnp.concatenate([top, side], axis=1), jnp.concatenate([side.T, low], axis=1)], axis=0
    )


def operator_apply(current, local_tiles, local_cols, halo_tiles, halo_slot, boundary):
    rounded = current.astype(jnp.bfloat16)
    outgoing = rounded[boundary]
    from_xlow = from_behind(outgoing[0], "px", 1)
    from_xhigh = from_behind(outgoing[1], "px", -1)
    from_ylow = from_behind(outgoing[2], "py", 1)
    from_yhigh = from_behind(outgoing[3], "py", -1)
    received = jnp.concatenate([from_xlow, from_xhigh, from_ylow, from_yhigh], axis=0)
    gathered = rounded[local_cols]
    product = jnp.einsum(
        "rtkj,rtij->rki", gathered, local_tiles, preferred_element_type=jnp.float32
    )
    coupled = jnp.einsum(
        "rkj,rij->rki", received[halo_slot], halo_tiles, preferred_element_type=jnp.float32
    )
    return product + coupled


def shards(start_vecs, local_tiles, local_cols, halo_tiles, halo_slot, boundary):

    def step_apply(current):
        return operator_apply(current, local_tiles, local_cols, halo_tiles, halo_slot, boundary)

    first_vecs = step_apply(start_vecs)

    def advance(step_index, state_pair):
        older_vec, newer_vec = state_pair
        return (newer_vec, 2.0 * step_apply(newer_vec) - older_vec)

    previous, current = lax.fori_loop(0, DEG - 1, advance, (start_vecs, first_vecs))
    total_rows = current.shape[0] * current.shape[2] * lax.axis_size("px") * lax.axis_size("py")
    partial_gram = jnp.einsum("rkj,rlj->kl", current, current, precision=lax.Precision.HIGHEST)
    raw_gram = unfold_symmetric(gathered_sum(fold_symmetric(partial_gram), ("px", "py")))
    squares = jnp.diagonal(raw_gram)
    scales = lax.rsqrt(squares / total_rows + 1e-06)
    filtered = current * scales[None, :, None]
    gram_matrix = raw_gram * scales[:, None] * scales[None, :] / total_rows
    return (filtered, gram_matrix)


def solution(mesh):
    return jax.shard_map(
        shards,
        mesh=mesh,
        in_specs=(
            P(("px", "py"), None, None),
            P(("px", "py"), None, None, None),
            P(("px", "py"), None),
            P(("px", "py"), None, None),
            P(("px", "py")),
            P(("px", "py"), None),
        ),
        out_specs=(P(("px", "py"), None, None), P()),
        check_vma=False,
    )
```

```python
import jax
import jax.numpy as jnp
from jax import lax
from jax.sharding import PartitionSpec as P

DEG = 9


def from_behind(value, axis, steps):
    count = lax.axis_size(axis)
    pairs = [(source, (source + steps) % count) for source in range(count)]
    return lax.ppermute(value, axis, pairs)


def gathered_sum(value, axis):
    return jnp.sum(lax.all_gather(value, axis), axis=0)


def operator_apply(current, local_tiles, local_cols, halo_tiles, halo_slot, boundary):
    rounded = current.astype(jnp.bfloat16)
    outgoing = rounded[boundary]
    from_xlow = from_behind(outgoing[0], "px", 1)
    from_xhigh = from_behind(outgoing[1], "px", -1)
    from_ylow = from_behind(outgoing[2], "py", 1)
    from_yhigh = from_behind(outgoing[3], "py", -1)
    received = jnp.concatenate([from_xlow, from_xhigh, from_ylow, from_yhigh], axis=0)
    gathered = rounded[local_cols]
    product = jnp.einsum(
        "rtkj,rtij->rki", gathered, local_tiles, preferred_element_type=jnp.float32
    )
    coupled = jnp.einsum(
        "rkj,rij->rki", received[halo_slot], halo_tiles, preferred_element_type=jnp.float32
    )
    return product + coupled


def shards(start_vecs, local_tiles, local_cols, halo_tiles, halo_slot, boundary):

    def step_apply(current):
        return operator_apply(current, local_tiles, local_cols, halo_tiles, halo_slot, boundary)

    first_vecs = step_apply(start_vecs)

    def advance(step_index, state_pair):
        older_vec, newer_vec = state_pair
        return (newer_vec, 2.0 * step_apply(newer_vec) - older_vec)

    previous, current = lax.fori_loop(0, DEG - 1, advance, (start_vecs, first_vecs))
    total_rows = current.shape[0] * current.shape[2] * lax.axis_size("px") * lax.axis_size("py")
    partial_gram = jnp.einsum("rkj,rlj->kl", current, current, precision=lax.Precision.HIGHEST)
    raw_gram = gathered_sum(gathered_sum(partial_gram, "px"), "py")
    squares = jnp.diagonal(raw_gram)
    scales = lax.rsqrt(squares / total_rows + 1e-06)
    filtered = current * scales[None, :, None]
    gram_matrix = raw_gram * scales[:, None] * scales[None, :] / total_rows
    return (filtered, gram_matrix)


def solution(mesh):
    return jax.shard_map(
        shards,
        mesh=mesh,
        in_specs=(
            P(("px", "py"), None, None),
            P(("px", "py"), None, None, None),
            P(("px", "py"), None),
            P(("px", "py"), None, None),
            P(("px", "py")),
            P(("px", "py"), None),
        ),
        out_specs=(P(("px", "py"), None, None), P()),
        check_vma=False,
    )
```
